256 devices in a mesh: seq: 8 (over x_hi, y), exp: 32 (over x_lo, z, core).
Axes of the slice: x: 4 (x_hi: 2, x_lo: 2; x = x_hi * 2 + x_lo), y: 4, z: 8, core: 2. Of those that a mesh axis runs over, the one named last changes fastest.
Arguments:
- tokens: bfloat16 [8192, 2560], P('exp'), may hold values from -6 to 6
- norm_gain: float32 [2560], replicated, may hold values from 0.1 to 1.9
- routes: int32 [8192, 6], P('exp'), may hold values from 0 to 63, all different within a row; in each aligned block of 256 rows (0 to 255, 256 to 511, ...) at most 25 rows name the same one
- route_weights: bfloat16 [8192, 6], P('exp'), may hold values from 0.049804688 to 0.3984375
- w_gate: bfloat16 [64, 2560, 1536], P('exp', None, 'seq'), may hold values from -0.125 to 0.125
- w_up: bfloat16 [64, 2560, 1536], P('exp', None, 'seq'), may hold values from -0.125 to 0.125
- w_down: bfloat16 [64, 1536, 2560], P('exp', 'seq'), may hold values from -0.15625 to 0.15625
- kv_prefill: bfloat16 [4, 2048, 32, 1024], P(None, ('seq', 'exp')), may hold values from -6 to 6
- block_map: int32 [2048], P(('seq', 'exp')), may hold values from 0 to 2047, as said below
- block_empty: int32 [2048], P(('seq', 'exp')), may hold values 0 or 1
Outputs:
- moe_out: bfloat16 [8192, 2560], P('exp', 'seq')
- kv_decode: bfloat16 [4, 2048, 32, 1024], P(None, ('seq', 'exp'))
The draws below stay inside these ranges and needn't reach their ends.
Inputs may be any that keep to these rules, and one draw needn't show every extreme that they name: `routes`: in each aligned block of 256 rows no expert is named by more than 25 rows, a bound that some block reaches. block_map is a permutation of the 2048 blocks; a block keeps its index of exp, and each device sends exactly 1 block to each device of its seq group, itself included.
All inputs are finite; a program needn't handle non-finite values. No bound on the sum of `block_empty` on one device may be relied on, other than what follows from the above.
Results may differ from the reference program's by a relative error of at most 0.013.
Values may be sent and summed in bfloat16 or wider, within the bound.
No kernel may reach another device: no remote copies, remote signals or barrier semaphores. Data moves between devices by JAX's collectives and lax.ppermute only.
A program may use at most 128 MiB of HBM per device.

```python
import math
import jax
import jax.numpy as jnp
import numpy as np
from jax import lax

D = 2560
FF = 1536
TOPK = 6
TOK_DEV = 256
LAYERS_KV = 4
BLK_TOK = 32
BLK_DEV = 8
EXPERTS = 64
CAP = 25
TOKENS = 8192
KVW = 1024
NBLK = 2048
N_SEQ = 8
N_EXP = 32


def draw_block_map(key, part):
    device_count = N_SEQ * N_EXP
    first_key, second_key = jax.random.split(jax.random.fold_in(key, 17))
    source_order = jax.vmap(lambda k: jax.random.permutation(k, BLK_DEV))(jax.random.split(first_key, device_count)).astype(jnp.int32)
    target_order = jax.vmap(lambda k: jax.random.permutation(k, BLK_DEV))(jax.random.split(second_key, device_count)).astype(jnp.int32)
    device = jnp.arange(device_count, dtype=jnp.int32)[:, None]
    ordinal = jnp.arange(BLK_DEV, dtype=jnp.int32)[None, :]
    seq_index = device // N_EXP
    exp_index = device % N_EXP
    target_seq = (seq_index + ordinal) % N_SEQ
    target_device = target_seq * N_EXP + exp_index
    target_slot = target_order[target_device, jnp.broadcast_to(ordinal, target_device.shape)]
    target = target_device * BLK_DEV + target_slot
    source = device * BLK_DEV + source_order
    result = jnp.zeros((device_count * BLK_DEV,), jnp.int32)
    return result.at[source.reshape(-1)].set(target.reshape(-1))


def touch_ends(entries, key, low, high):
    longest = entries.shape.index(max(entries.shape))
    spots = []
    for shift in (0, 1):
        where = [jax.random.randint(jax.random.fold_in(key, axis), (), 0, length) for axis, length in enumerate(entries.shape)]
        where[longest] = (where[longest] + shift) % entries.shape[longest]
        spots.append(tuple(where))
    return entries.at[spots[0]].set(low).at[spots[1]].set(high)


def level_of(rng, dims, cuts, low, high):
    def one(axis_at, parts):
        draws = jax.random.uniform(jax.random.fold_in(jax.random.fold_in(rng, 6), axis_at), (parts,), jnp.float32, low / len(cuts), high / len(cuts))
        return jnp.repeat(jnp.exp(draws), dims[axis_at] // parts).reshape((-1,) + (1,) * (len(dims) - axis_at - 1))

    gain = one(*cuts[0])
    for cut in cuts[1:]:
        gain = gain * one(*cut)
    return gain


def deal_out(stream_key, own, number, rows, amount, top, reach, skew):
    order = jax.random.permutation(stream_key, amount)
    heavy_load, common = portions_of(amount, rows * top, reach, skew, True), portions_of(amount, rows * top, reach, skew, False)
    places = jnp.arange(amount)

    def named(lengths, turn):
        used = int((lengths > 0).sum())
        fixed = max(1, used // 4)
        shifted = fixed + (places - fixed + turn * (used - fixed)) % max(1, amount - fixed)
        return jnp.zeros((amount,), jnp.int32).at[order[jnp.where(places < fixed, places, shifted)]].set(jnp.asarray(lengths, jnp.int32))

    lengths = jnp.where(number % 4 == 0, named(heavy_load, number // 4), named(common, number - number // 4 - 1))
    mixed = jax.random.permutation(jax.random.fold_in(own, 3), amount)
    source_of, sink = mixed[0:amount // 2 * 2:2], mixed[1:amount // 2 * 2:2]
    slack = jnp.minimum(lengths[source_of] - 1, reach - lengths[sink]) // 2
    slack = jnp.where((source_of == order[0]) | (sink == order[0]) | (lengths[sink] == 0), 0, jnp.maximum(slack, 0))
    shifted = jax.random.randint(jax.random.fold_in(own, 4), (amount // 2,), 0, 1 << 20) % (slack + 1)
    lengths = lengths.at[source_of].add(-shifted).at[sink].add(shifted)
    members = jnp.searchsorted(jnp.cumsum(lengths), jnp.arange(rows * top), side="right").astype(jnp.int32)
    table = members.reshape(top, rows).T
    table = table[jax.random.permutation(jax.random.fold_in(own, 1), rows)]
    turn = jax.random.randint(jax.random.fold_in(own, 2), (rows, 1), 0, top)
    return jnp.take_along_axis(table, (jnp.arange(top)[None, :] + turn) % top, axis=1)


def portions_of(count, total, limit, lean, full):
    weights = [(1 << 20) // math.isqrt(rank ** lean) + 1 for rank in range(1, count + 1)]
    largest = limit if full else min(limit, max(-(-total // count), total * weights[0] // sum(weights)))
    least = 1 if total - largest >= count - 1 else 0
    holding, spare = [largest] + [least] * (count - 1), total - largest - least * (count - 1)
    while spare > 0:
        movable = [i for i in range(1, count) if holding[i] < largest] or [i for i in range(1, count) if holding[i] < limit]
        mass, remaining = sum([weights[i] for i in movable]), spare
        for i in movable:
            addition = min(limit - holding[i], max(1, remaining * weights[i] // mass), spare)
            holding[i] = holding[i] + addition
            spare = spare - addition
    return np.array(holding)


def centred(stream_key, shape, width, limit, cuts=(), kind=jnp.bfloat16):
    gain = level_of(stream_key, shape, cuts, -0.22, 0.18) if cuts else 1.0
    values = jax.random.normal(stream_key, shape, jnp.float32) * width * gain
    return jnp.minimum(jnp.maximum(values, -limit), limit).astype(kind)


def setup_inputs(seed: int = 0) -> dict:
    arg_keys = jax.random.split(jax.random.key(seed), 11)
    tokens = centred(arg_keys[0], (TOKENS, D), 1.0, 6.0, ((0, 32),))
    norm_gain = jnp.clip(1.0 + 0.18 * jax.random.normal(arg_keys[1], (D,), jnp.float32), 0.1, 1.9)
    routes_keys = jax.random.split(jax.random.fold_in(arg_keys[2], 1), TOKENS // TOK_DEV)
    routes_turns = jax.random.permutation(jax.random.fold_in(arg_keys[2], 3), TOKENS // TOK_DEV)
    routes = jax.vmap(lambda own, number: deal_out(jax.random.fold_in(arg_keys[2], 2), own, number, TOK_DEV, EXPERTS, TOPK, CAP, 2))(routes_keys, routes_turns).reshape((TOKENS, TOPK))
    route_weights = jnp.clip(0.049804688 + 0.3486328 * jax.random.uniform(arg_keys[3], (TOKENS, TOPK), jnp.float32) ** level_of(arg_keys[3], (TOKENS, TOPK), ((0, 32),), -0.2, 0.2), 0.049804688, 0.3984375).astype(jnp.bfloat16)
    w_gate = centred(arg_keys[4], (EXPERTS, D, FF), D ** -0.5, 0.125, ((0, 32), (2, 8)))
    w_up = centred(arg_keys[5], (EXPERTS, D, FF), D ** -0.5, 0.125, ((0, 32), (2, 8)))
    w_down = centred(arg_keys[6], (EXPERTS, FF, D), FF ** -0.5, 0.15625, ((0, 32), (1, 8)))
    kv_prefill = centred(arg_keys[7], (LAYERS_KV, NBLK, BLK_TOK, KVW), 1.0, 6.0, ((1, 256),))
    block_map = draw_block_map(jax.random.fold_in(arg_keys[10], 71), 0)
    block_empty = touch_ends((jax.random.randint(arg_keys[9], (NBLK,), 0, 4) < 1).astype(jnp.int32), jax.random.fold_in(arg_keys[9], 1), 0, 1)
    return {"tokens": tokens, "norm_gain": norm_gain, "routes": routes, "route_weights": route_weights, "w_gate": w_gate, "w_up": w_up, "w_down": w_down, "kv_prefill": kv_prefill, "block_map": block_map, "block_empty": block_empty}


def reference(tokens, norm_gain, routes, route_weights, w_gate, w_up, w_down, kv_prefill, block_map, block_empty):
    values = tokens.astype(jnp.float32)
    scale = lax.rsqrt(lax.optimization_barrier(jnp.mean(values * values, axis=-1, keepdims=True)) + 1e-06)
    normed = (values * scale * norm_gain).astype(jnp.bfloat16)
    assigned = TOKENS * TOPK
    most_rows = CAP * N_EXP
    slice_width = FF // N_SEQ
    flat_routes = routes.reshape(-1)
    weight_table = jnp.concatenate([route_weights.reshape(-1).astype(jnp.float32), jnp.zeros((1,), jnp.float32)])
    padded = jnp.concatenate([normed, jnp.zeros((1, D), jnp.bfloat16)], axis=0)

    def one_expert(totals, expert):
        index = jnp.nonzero(flat_routes == expert, size=most_rows, fill_value=assigned)[0].astype(jnp.int32)
        token_index = index // TOPK
        rows = padded[token_index]
        gate = jnp.dot(rows, w_gate[expert], preferred_element_type=jnp.float32)
        upward = jnp.dot(rows, w_up[expert], preferred_element_type=jnp.float32)
        hidden = (jax.nn.silu(gate) * upward).astype(jnp.bfloat16)
        pieces = jnp.einsum('rsf,sfd->rsd', hidden.reshape(most_rows, N_SEQ, slice_width).astype(jnp.float32), w_down[expert].reshape(N_SEQ, slice_width, D).astype(jnp.float32), precision=lax.Precision.HIGHEST)
        rounded = lax.optimization_barrier(pieces.astype(jnp.bfloat16))
        expert_out = lax.optimization_barrier(jnp.sum(rounded.astype(jnp.float32), axis=1))
        weight = weight_table[index]
        totals = totals.at[token_index].add(expert_out * weight[:, None])
        return (totals, None)
    start = jnp.zeros((TOKENS + 1, D), jnp.float32)
    totals, unused = lax.scan(one_expert, start, jnp.arange(EXPERTS, dtype=jnp.int32))
    moe_out = totals[:TOKENS].astype(jnp.bfloat16)
    keep = (1 - block_empty).astype(kv_prefill.dtype)
    kept = kv_prefill * keep[None, :, None, None]
    kv_decode = jnp.zeros_like(kept).at[:, block_map].set(kept)
    return (moe_out, kv_decode)
```

```python
import jax
import jax.numpy as jnp
from jax import lax
from jax.sharding import PartitionSpec as P


def rms_normed(tokens, norm_gain):
    values = tokens.astype(jnp.float32)
    scale = lax.rsqrt(jnp.mean(values * values, axis=-1, keepdims=True) + 1e-06)
    return (values * scale * norm_gain).astype(jnp.bfloat16)


def route_positions(routes, experts):
    tok_count = routes.shape[0]
    expert_ids = jnp.arange(experts, dtype=jnp.int32)
    onehot = routes[:, :, None] == expert_ids[None, None, :]
    member = jnp.any(onehot, axis=1).astype(jnp.bfloat16)
    rows = jnp.arange(tok_count, dtype=jnp.int32)
    earlier = (rows[None, :] < rows[:, None]).astype(jnp.bfloat16)
    counts = jnp.dot(earlier, member, preferred_element_type=jnp.float32)
    picked = jnp.sum(jnp.where(onehot, counts[:, None, :], 0.0), axis=2)
    return picked.astype(jnp.int32)


def expert_block(rows, w_gate, w_up, w_down):
    gate = jnp.einsum("erd,edf->erf", rows, w_gate, preferred_element_type=jnp.float32)
    upward = jnp.einsum("erd,edf->erf", rows, w_up, preferred_element_type=jnp.float32)
    hidden = (jax.nn.silu(gate) * upward).astype(jnp.bfloat16)
    return jnp.einsum("erf,efd->erd", hidden, w_down, preferred_element_type=jnp.float32).astype(
        jnp.bfloat16
    )


def relayout(kv_prefill, block_map, block_empty):
    layers, blocks, block_rows, kv_width = kv_prefill.shape
    exp_count = lax.axis_size("exp")
    keep = (1 - block_empty).astype(kv_prefill.dtype)
    peer = block_map // blocks // exp_count
    target = block_map % blocks
    order = jnp.argsort(peer)
    outgoing = kv_prefill[:, order] * keep[order][None, :, None, None]
    labels = target[order]
    arrived = lax.all_to_all(outgoing, "seq", split_axis=1, concat_axis=1, tiled=True)
    slots = lax.all_to_all(labels, "seq", split_axis=0, concat_axis=0, tiled=True)
    return arrived[:, jnp.argsort(slots)]


def per_device(
    tokens,
    norm_gain,
    routes,
    route_weights,
    w_gate,
    w_up,
    w_down,
    kv_prefill,
    block_map,
    block_empty,
):
    local_experts = w_gate.shape[0]
    exp_count = lax.axis_size("exp")
    seq_count = lax.axis_size("seq")
    experts = local_experts * exp_count
    tok_count, topk = routes.shape
    capacity = tok_count * topk // experts + 1
    seq_per_expert = seq_count // local_experts
    per_dev = -(-capacity // seq_per_expert)
    my_seq = lax.axis_index("seq")

    normed = rms_normed(tokens, norm_gain)
    width = normed.shape[1]

    position = route_positions(routes, experts)
    owner = routes // local_experts
    local_index = routes % local_experts
    sender = local_index * seq_per_expert + position // per_dev
    within = position % per_dev

    send_slots = exp_count * per_dev
    slot_of = jnp.where(sender == my_seq, owner * per_dev + within, -1)
    slot_ids = jnp.arange(send_slots, dtype=jnp.int32)
    pick = jnp.any(slot_of[None, :, :] == slot_ids[:, None, None], axis=2).astype(jnp.bfloat16)
    outgoing = jnp.dot(pick, normed, preferred_element_type=jnp.float32).astype(jnp.bfloat16)
    outgoing = outgoing.reshape(exp_count, per_dev, width)
    arrived = lax.all_to_all(outgoing, "exp", split_axis=0, concat_axis=0, tiled=True)
    gathered = lax.all_gather(arrived, "seq", axis=0, tiled=False)
    rows = gathered.reshape(local_experts, seq_per_expert * exp_count * per_dev, width)

    partial_value = expert_block(rows, w_gate, w_up, w_down)
    summed = lax.psum_scatter(partial_value, "seq", scatter_dimension=2, tiled=True)
    part_width = summed.shape[2]
    summed = summed.reshape(local_experts, seq_per_expert, exp_count, per_dev, part_width)
    summed = jnp.transpose(summed, (2, 0, 1, 3, 4))
    returned = lax.all_to_all(summed, "exp", split_axis=0, concat_axis=0, tiled=True)
    recv_slots = exp_count * seq_count * per_dev
    returned = returned.reshape(recv_slots, part_width)

    recv_slot = (owner * seq_count + sender) * per_dev + within
    recv_ids = jnp.arange(recv_slots, dtype=jnp.int32)
    weights = route_weights.astype(jnp.float32)
    mix = jnp.sum(
        jnp.where(recv_slot[:, :, None] == recv_ids[None, None, :], weights[:, :, None], 0.0), axis=1
    ).astype(jnp.bfloat16)
    mixed = jnp.dot(mix, returned, preferred_element_type=jnp.float32).astype(jnp.bfloat16)

    kv_decode = relayout(kv_prefill, block_map, block_empty)
    return (mixed, kv_decode)


def solution(mesh):
    in_specs = (
        P("exp", None),
        P(),
        P("exp", None),
        P("exp", None),
        P("exp", None, "seq"),
        P("exp", None, "seq"),
        P("exp", "seq", None),
        P(None, ("seq", "exp"), None, None),
        P(("seq", "exp")),
        P(("seq", "exp")),
    )
    out_specs = (P("exp", "seq"), P(None, ("seq", "exp"), None, None))
    return jax.shard_map(
        per_device, mesh=mesh, in_specs=in_specs, out_specs=out_specs, check_vma=False
    )
```

```python
import jax
import jax.numpy as jnp
from jax import lax
from jax.sharding import PartitionSpec as P


def rms_normed(tokens, norm_gain):
    values = tokens.astype(jnp.float32)
    scale = lax.rsqrt(jnp.mean(values * values, axis=-1, keepdims=True) + 1e-06)
    return (values * scale * norm_gain).astype(jnp.bfloat16)


def route_positions(routes, experts):
    tok_count = routes.shape[0]
    expert_ids = jnp.arange(experts, dtype=jnp.int32)
    onehot = routes[:, :, None] == expert_ids[None, None, :]
    member = jnp.any(onehot, axis=1).astype(jnp.bfloat16)
    rows = jnp.arange(tok_count, dtype=jnp.int32)
    earlier = (rows[None, :] < rows[:, None]).astype(jnp.bfloat16)
    counts = jnp.dot(earlier, member, preferred_element_type=jnp.float32)
    picked = jnp.sum(jnp.where(onehot, counts[:, None, :], 0.0), axis=2)
    return picked.astype(jnp.int32)


def relayout(kv_prefill, block_map, block_empty):
    layers, blocks, block_rows, kv_width = kv_prefill.shape
    exp_count = lax.axis_size("exp")
    keep = (1 - block_empty).astype(kv_prefill.dtype)
    peer = block_map // blocks // exp_count
    target = block_map % blocks
    order = jnp.argsort(peer)
    outgoing = kv_prefill[:, order] * keep[order][None, :, None, None]
    labels = target[order]
    arrived = lax.all_to_all(outgoing, "seq", split_axis=1, concat_axis=1, tiled=True)
    slots = lax.all_to_all(labels, "seq", split_axis=0, concat_axis=0, tiled=True)
    return arrived[:, jnp.argsort(slots)]


def per_device(
    tokens,
    norm_gain,
    routes,
    route_weights,
    w_gate,
    w_up,
    w_down,
    kv_prefill,
    block_map,
    block_empty,
):
    local_experts = w_gate.shape[0]
    exp_count = lax.axis_size("exp")
    seq_count = lax.axis_size("seq")
    experts = local_experts * exp_count
    tok_count, topk = routes.shape
    capacity = tok_count * topk // experts + 1
    seq_per_expert = seq_count // local_experts
    per_dev = -(-capacity // seq_per_expert)
    my_seq = lax.axis_index("seq")

    normed = rms_normed(tokens, norm_gain)
    width = normed.shape[1]

    position = route_positions(routes, experts)
    owner = routes // local_experts
    local_index = routes % local_experts
    sender = local_index * seq_per_expert + position // per_dev
    within = position % per_dev

    send_slots = per_dev * exp_count
    slot_of = jnp.where(sender == my_seq, within * exp_count + owner, -1)
    slot_ids = jnp.arange(send_slots, dtype=jnp.int32)
    pick = jnp.any(slot_of[None, :, :] == slot_ids[:, None, None], axis=2).astype(jnp.bfloat16)
    outgoing = jnp.dot(pick, normed, preferred_element_type=jnp.float32).astype(jnp.bfloat16)
    outgoing = outgoing.reshape(per_dev, exp_count, width)
    arrived = lax.all_to_all(outgoing, "exp", split_axis=1, concat_axis=1, tiled=True)
    copies = jnp.broadcast_to(arrived[None], (seq_count,) + arrived.shape)
    gathered = lax.all_to_all(copies, "seq", split_axis=0, concat_axis=0, tiled=True)
    rows = gathered.reshape(local_experts, seq_per_expert * per_dev * exp_count, width)

    gate = jnp.einsum("erd,edf->erf", rows, w_gate, preferred_element_type=jnp.float32)
    upward = jnp.einsum("erd,edf->erf", rows, w_up, preferred_element_type=jnp.float32)
    hidden = (jax.nn.silu(gate) * upward).astype(jnp.bfloat16)
    part_width = width // seq_count
    down = w_down.reshape(local_experts, w_down.shape[1], seq_count, part_width)
    partial_value = jnp.einsum(
        "erf,efcd->cerd", hidden, down, preferred_element_type=jnp.float32
    ).astype(jnp.bfloat16)
    pieces = lax.all_to_all(partial_value, "seq", split_axis=0, concat_axis=0, tiled=True)
    summed = jnp.sum(pieces.astype(jnp.float32), axis=0).astype(jnp.bfloat16)
    summed = summed.reshape(seq_count * per_dev, exp_count, part_width)
    returned = lax.all_to_all(summed, "exp", split_axis=1, concat_axis=1, tiled=True)
    recv_slots = seq_count * per_dev * exp_count
    returned = returned.reshape(recv_slots, part_width)

    recv_slot = (sender * per_dev + within) * exp_count + owner
    recv_ids = jnp.arange(recv_slots, dtype=jnp.int32)
    weights = route_weights.astype(jnp.float32)
    mix = jnp.sum(
        jnp.where(recv_slot[:, :, None] == recv_ids[None, None, :], weights[:, :, None], 0.0), axis=1
    ).astype(jnp.bfloat16)
    mixed = jnp.dot(mix, returned, preferred_element_type=jnp.float32).astype(jnp.bfloat16)

    kv_decode = relayout(kv_prefill, block_map, block_empty)
    return (mixed, kv_decode)


def solution(mesh):
    in_specs = (
        P("exp", None),
        P(),
        P("exp", None),
        P("exp", None),
        P("exp", None, "seq"),
        P("exp", None, "seq"),
        P("exp", "seq", None),
        P(None, ("seq", "exp"), None, None),
        P(("seq", "exp")),
        P(("seq", "exp")),
    )
    out_specs = (P("exp", "seq"), P(None, ("seq", "exp"), None, None))
    return jax.shard_map(
        per_device, mesh=mesh, in_specs=in_specs, out_specs=out_specs, check_vma=False
    )
```

```python
import jax
import jax.numpy as jnp
from jax import lax
from jax.sharding import PartitionSpec as P


def rms_normed(tokens, norm_gain):
    values = tokens.astype(jnp.float32)
    scale = lax.rsqrt(jnp.mean(values * values, axis=-1, keepdims=True) + 1e-06)
    return (values * scale * norm_gain).astype(jnp.bfloat16)


def route_positions(routes, experts):
    tok_count = routes.shape[0]
    expert_ids = jnp.arange(experts, dtype=jnp.int32)
    onehot = routes[:, :, None] == expert_ids[None, None, :]
    member = jnp.any(onehot, axis=1).astype(jnp.bfloat16)
    rows = jnp.arange(tok_count, dtype=jnp.int32)
    earlier = (rows[None, :] < rows[:, None]).astype(jnp.bfloat16)
    counts = jnp.dot(earlier, member, preferred_element_type=jnp.float32)
    picked = jnp.sum(jnp.where(onehot, counts[:, None, :], 0.0), axis=2)
    return picked.astype(jnp.int32)


def relayout_outgoing(kv_prefill, block_map, block_empty):
    layers, blocks, block_rows, kv_width = kv_prefill.shape
    exp_count = lax.axis_size("exp")
    keep = (1 - block_empty).astype(kv_prefill.dtype)
    peer = block_map // blocks // exp_count
    target = block_map % blocks
    order = jnp.argsort(peer)
    return kv_prefill[:, order] * keep[order][None, :, None, None], target[order]


def relayout_exchange(outgoing, labels):
    arrived = lax.all_to_all(outgoing, "seq", split_axis=1, concat_axis=1, tiled=True)
    slots = lax.all_to_all(labels, "seq", split_axis=0, concat_axis=0, tiled=True)
    return arrived[:, jnp.argsort(slots)]


def per_device(
    tokens,
    norm_gain,
    routes,
    route_weights,
    w_gate,
    w_up,
    w_down,
    kv_prefill,
    block_map,
    block_empty,
):
    local_experts = w_gate.shape[0]
    exp_count = lax.axis_size("exp")
    seq_count = lax.axis_size("seq")
    experts = local_experts * exp_count
    tok_count, topk = routes.shape
    capacity = tok_count * topk // experts + 1
    seq_per_expert = seq_count // local_experts
    per_dev = -(-capacity // seq_per_expert)
    my_seq = lax.axis_index("seq")

    normed = rms_normed(tokens, norm_gain)
    width = normed.shape[1]

    position = route_positions(routes, experts)
    owner = routes // local_experts
    local_index = routes % local_experts
    sender = local_index * seq_per_expert + position // per_dev
    within = position % per_dev

    send_slots = per_dev * exp_count
    slot_of = jnp.where(sender == my_seq, within * exp_count + owner, -1)
    slot_ids = jnp.arange(send_slots, dtype=jnp.int32)
    pick = jnp.any(slot_of[None, :, :] == slot_ids[:, None, None], axis=2).astype(jnp.bfloat16)
    outgoing = jnp.dot(pick, normed, preferred_element_type=jnp.float32).astype(jnp.bfloat16)
    outgoing = outgoing.reshape(per_dev, exp_count, width)
    arrived = lax.all_to_all(outgoing, "exp", split_axis=1, concat_axis=1, tiled=True)
    copies = jnp.broadcast_to(arrived[None], (seq_count,) + arrived.shape)
    gathered = lax.all_to_all(copies, "seq", split_axis=0, concat_axis=0, tiled=True)
    kv_out, kv_labels = relayout_outgoing(kv_prefill, block_map, block_empty)
    gathered, kv_out, kv_labels = lax.optimization_barrier((gathered, kv_out, kv_labels))
    rows = gathered.reshape(local_experts, seq_per_expert * per_dev * exp_count, width)

    gate = jnp.einsum("erd,edf->erf", rows, w_gate, preferred_element_type=jnp.float32)
    upward = jnp.einsum("erd,edf->erf", rows, w_up, preferred_element_type=jnp.float32)
    hidden = (jax.nn.silu(gate) * upward).astype(jnp.bfloat16)
    part_width = width // seq_count
    down = w_down.reshape(local_experts, w_down.shape[1], seq_count, part_width)
    partial_value = jnp.einsum(
        "erf,efcd->cerd", hidden, down, preferred_element_type=jnp.float32
    ).astype(jnp.bfloat16)
    kv_decode = relayout_exchange(kv_out, kv_labels)
    kv_decode, partial_value = lax.optimization_barrier((kv_decode, partial_value))
    pieces = lax.all_to_all(partial_value, "seq", split_axis=0, concat_axis=0, tiled=True)
    summed = jnp.sum(pieces.astype(jnp.float32), axis=0).astype(jnp.bfloat16)
    summed = summed.reshape(seq_count * per_dev, exp_count, part_width)
    returned = lax.all_to_all(summed, "exp", split_axis=1, concat_axis=1, tiled=True)
    recv_slots = seq_count * per_dev * exp_count
    returned = returned.reshape(recv_slots, part_width)

    recv_slot = (sender * per_dev + within) * exp_count + owner
    recv_ids = jnp.arange(recv_slots, dtype=jnp.int32)
    weights = route_weights.astype(jnp.float32)
    mix = jnp.sum(
        jnp.where(recv_slot[:, :, None] == recv_ids[None, None, :], weights[:, :, None], 0.0), axis=1
    ).astype(jnp.bfloat16)
    mixed = jnp.dot(mix, returned, preferred_element_type=jnp.float32).astype(jnp.bfloat16)

    return (mixed, kv_decode)


def solution(mesh):
    in_specs = (
        P("exp", None),
        P(),
        P("exp", None),
        P("exp", None),
        P("exp", None, "seq"),
        P("exp", None, "seq"),
        P("exp", "seq", None),
        P(None, ("seq", "exp"), None, None),
        P(("seq", "exp")),
        P(("seq", "exp")),
    )
    out_specs = (P("exp", "seq"), P(None, ("seq", "exp"), None, None))
    return jax.shard_map(
        per_device, mesh=mesh, in_specs=in_specs, out_specs=out_specs, check_vma=False
    )
```

```python
import jax
import jax.numpy as jnp
from jax import lax
from jax.sharding import PartitionSpec as P


def rms_normed(tokens, norm_gain):
    values = tokens.astype(jnp.float32)
    scale = lax.rsqrt(jnp.mean(values * values, axis=-1, keepdims=True) + 1e-06)
    return (values * scale * norm_gain).astype(jnp.bfloat16)


def route_positions(routes, experts):
    tok_count = routes.shape[0]
    expert_ids = jnp.arange(experts, dtype=jnp.int32)
    onehot = routes[:, :, None] == expert_ids[None, None, :]
    member = jnp.any(onehot, axis=1).astype(jnp.bfloat16)
    rows = jnp.arange(tok_count, dtype=jnp.int32)
    earlier = (rows[None, :] < rows[:, None]).astype(jnp.bfloat16)
    counts = jnp.dot(earlier, member, preferred_element_type=jnp.float32)
    picked = jnp.sum(jnp.where(onehot, counts[:, None, :], 0.0), axis=2)
    return picked.astype(jnp.int32)


def relayout_outgoing(kv_prefill, block_map, block_empty):
    layers, blocks, block_rows, kv_width = kv_prefill.shape
    exp_count = lax.axis_size("exp")
    keep = (1 - block_empty).astype(kv_prefill.dtype)
    peer = block_map // blocks // exp_count
    target = block_map % blocks
    order = jnp.argsort(peer)
    return kv_prefill[:, order] * keep[order][None, :, None, None], target[order]


def relayout_exchange(outgoing, labels):
    arrived = lax.all_to_all(outgoing, "seq", split_axis=1, concat_axis=1, tiled=True)
    slots = lax.all_to_all(labels, "seq", split_axis=0, concat_axis=0, tiled=True)
    return arrived[:, jnp.argsort(slots)]


def per_device(
    tokens,
    norm_gain,
    routes,
    route_weights,
    w_gate,
    w_up,
    w_down,
    kv_prefill,
    block_map,
    block_empty,
):
    local_experts = w_gate.shape[0]
    exp_count = lax.axis_size("exp")
    seq_count = lax.axis_size("seq")
    experts = local_experts * exp_count
    tok_count, topk = routes.shape
    capacity = tok_count * topk // experts + 1
    seq_per_expert = seq_count // local_experts
    share = (capacity * 2) // (3 * seq_per_expert)
    direct = capacity - share * seq_per_expert
    my_seq = lax.axis_index("seq")

    normed = rms_normed(tokens, norm_gain)
    width = normed.shape[1]

    position = route_positions(routes, experts)
    owner = routes // local_experts
    local_index = routes % local_experts
    shared = position >= direct
    sender = local_index * seq_per_expert + (position - direct) // share
    within = (position - direct) % share

    direct_slots = local_experts * direct
    direct_of = jnp.where(shared, -1, (local_index * direct + position) * exp_count + owner)
    direct_ids = jnp.arange(direct_slots * exp_count, dtype=jnp.int32)
    pick = jnp.any(direct_of[None, :, :] == direct_ids[:, None, None], axis=2).astype(jnp.bfloat16)
    direct_rows = jnp.dot(pick, normed, preferred_element_type=jnp.float32).astype(jnp.bfloat16)
    direct_rows = direct_rows.reshape(direct_slots, exp_count, width)

    share_of = jnp.where(shared & (sender == my_seq), within * exp_count + owner, -1)
    share_ids = jnp.arange(share * exp_count, dtype=jnp.int32)
    pick = jnp.any(share_of[None, :, :] == share_ids[:, None, None], axis=2).astype(jnp.bfloat16)
    share_rows = jnp.dot(pick, normed, preferred_element_type=jnp.float32).astype(jnp.bfloat16)
    share_rows = share_rows.reshape(share, exp_count, width)

    share_arrived = lax.all_to_all(share_rows, "exp", split_axis=1, concat_axis=1, tiled=True)
    share_gathered = lax.all_gather(share_arrived, "seq", axis=0, tiled=False)
    direct_arrived = lax.all_to_all(direct_rows, "exp", split_axis=1, concat_axis=1, tiled=True)

    kv_out, kv_labels = relayout_outgoing(kv_prefill, block_map, block_empty)
    share_gathered, direct_arrived, kv_out, kv_labels = lax.optimization_barrier(
        (share_gathered, direct_arrived, kv_out, kv_labels)
    )
    share_gathered = share_gathered.reshape(
        local_experts, seq_per_expert * share, exp_count, width
    )
    direct_arrived = direct_arrived.reshape(local_experts, direct, exp_count, width)
    rows = jnp.concatenate([direct_arrived, share_gathered], axis=1).reshape(
        local_experts, capacity * exp_count, width
    )

    gate = jnp.einsum("erd,edf->erf", rows, w_gate, preferred_element_type=jnp.float32)
    upward = jnp.einsum("erd,edf->erf", rows, w_up, preferred_element_type=jnp.float32)
    hidden = (jax.nn.silu(gate) * upward).astype(jnp.bfloat16)
    part_width = width // seq_count
    down = w_down.reshape(local_experts, w_down.shape[1], seq_count, part_width)
    partial_value = jnp.einsum(
        "erf,efcd->cerd", hidden, down, preferred_element_type=jnp.float32
    ).astype(jnp.bfloat16)
    kv_decode = relayout_exchange(kv_out, kv_labels)
    kv_decode, partial_value = lax.optimization_barrier((kv_decode, partial_value))
    pieces = lax.all_to_all(partial_value, "seq", split_axis=0, concat_axis=0, tiled=True)
    summed = jnp.sum(pieces.astype(jnp.float32), axis=0).astype(jnp.bfloat16)
    summed = summed.reshape(local_experts * capacity, exp_count, part_width)
    returned = lax.all_to_all(summed, "exp", split_axis=1, concat_axis=1, tiled=True)
    recv_slots = local_experts * capacity * exp_count
    returned = returned.reshape(recv_slots, part_width)

    recv_slot = (local_index * capacity + position) * exp_count + owner
    recv_ids = jnp.arange(recv_slots, dtype=jnp.int32)
    weights = route_weights.astype(jnp.float32)
    mix = jnp.sum(
        jnp.where(recv_slot[:, :, None] == recv_ids[None, None, :], weights[:, :, None], 0.0), axis=1
    ).astype(jnp.bfloat16)
    mixed = jnp.dot(mix, returned, preferred_element_type=jnp.float32).astype(jnp.bfloat16)

    return (mixed, kv_decode)


def solution(mesh):
    in_specs = (
        P("exp", None),
        P(),
        P("exp", None),
        P("exp", None),
        P("exp", None, "seq"),
        P("exp", None, "seq"),
        P("exp", "seq", None),
        P(None, ("seq", "exp"), None, None),
        P(("seq", "exp")),
        P(("seq", "exp")),
    )
    out_specs = (P("exp", "seq"), P(None, ("seq", "exp"), None, None))
    return jax.shard_map(
        per_device, mesh=mesh, in_specs=in_specs, out_specs=out_specs, check_vma=False
    )
```

```python
import jax
import jax.numpy as jnp
from jax import lax
from jax.sharding import PartitionSpec as P


def rms_normed(tokens, norm_gain):
    values = tokens.astype(jnp.float32)
    scale = lax.rsqrt(jnp.mean(values * values, axis=-1, keepdims=True) + 1e-06)
    return (values * scale * norm_gain).astype(jnp.bfloat16)


def route_positions(routes, experts):
    tok_count = routes.shape[0]
    expert_ids = jnp.arange(experts, dtype=jnp.int32)
    onehot = routes[:, :, None] == expert_ids[None, None, :]
    member = jnp.any(onehot, axis=1).astype(jnp.bfloat16)
    rows = jnp.arange(tok_count, dtype=jnp.int32)
    earlier = (rows[None, :] < rows[:, None]).astype(jnp.bfloat16)
    counts = jnp.dot(earlier, member, preferred_element_type=jnp.float32)
    picked = jnp.sum(jnp.where(onehot, counts[:, None, :], 0.0), axis=2)
    return picked.astype(jnp.int32)


def relayout(kv_prefill, block_map, block_empty):
    layers, blocks, block_rows, kv_width = kv_prefill.shape
    seq_count = lax.axis_size("seq")
    exp_count = lax.axis_size("exp")
    my_seq = lax.axis_index("seq")
    keep = (1 - block_empty).astype(kv_prefill.dtype)
    peer = block_map // blocks // exp_count
    target = block_map % blocks
    order = jnp.argsort((peer - my_seq) % seq_count)
    outgoing = kv_prefill[:, order] * keep[order][None, :, None, None]
    labels = target[order]
    pieces = [outgoing[:, 0]]
    tags = [labels[0]]
    for step in range(1, seq_count):
        route = [(i, (i + step) % seq_count) for i in range(seq_count)]
        piece, tag = lax.ppermute((outgoing[:, step], labels[step]), "seq", route)
        pieces.append(piece)
        tags.append(tag)
    return jnp.stack(pieces, axis=1), jnp.stack(tags)


def per_device(
    tokens,
    norm_gain,
    routes,
    route_weights,
    w_gate,
    w_up,
    w_down,
    kv_prefill,
    block_map,
    block_empty,
):
    local_experts = w_gate.shape[0]
    exp_count = lax.axis_size("exp")
    seq_count = lax.axis_size("seq")
    experts = local_experts * exp_count
    tok_count, topk = routes.shape
    capacity = tok_count * topk // experts + 1
    seq_per_expert = seq_count // local_experts
    per_dev = -(-capacity // seq_per_expert)
    my_seq = lax.axis_index("seq")

    normed = rms_normed(tokens, norm_gain)
    width = normed.shape[1]

    position = route_positions(routes, experts)
    owner = routes // local_experts
    local_index = routes % local_experts
    sender = local_index * seq_per_expert + position // per_dev
    within = position % per_dev

    send_slots = per_dev * exp_count
    slot_of = jnp.where(sender == my_seq, within * exp_count + owner, -1)
    slot_ids = jnp.arange(send_slots, dtype=jnp.int32)
    pick = jnp.any(slot_of[None, :, :] == slot_ids[:, None, None], axis=2).astype(jnp.bfloat16)
    outgoing = jnp.dot(pick, normed, preferred_element_type=jnp.float32).astype(jnp.bfloat16)
    outgoing = outgoing.reshape(per_dev, exp_count, width)
    arrived = lax.all_to_all(outgoing, "exp", split_axis=1, concat_axis=1, tiled=True)
    kv_arrived, kv_slots = relayout(kv_prefill, block_map, block_empty)
    arrived, kv_arrived, kv_slots = lax.optimization_barrier((arrived, kv_arrived, kv_slots))
    copies = jnp.broadcast_to(arrived[None], (seq_count,) + arrived.shape)
    gathered = lax.all_to_all(copies, "seq", split_axis=0, concat_axis=0, tiled=True)
    rows = gathered.reshape(local_experts, seq_per_expert * per_dev * exp_count, width)

    gate = jnp.einsum("erd,edf->erf", rows, w_gate, preferred_element_type=jnp.float32)
    upward = jnp.einsum("erd,edf->erf", rows, w_up, preferred_element_type=jnp.float32)
    hidden = (jax.nn.silu(gate) * upward).astype(jnp.bfloat16)
    part_width = width // seq_count
    down = w_down.reshape(local_experts, w_down.shape[1], seq_count, part_width)
    partial_value = jnp.einsum(
        "erf,efcd->cerd", hidden, down, preferred_element_type=jnp.float32
    ).astype(jnp.bfloat16)
    pieces = lax.all_to_all(partial_value, "seq", split_axis=0, concat_axis=0, tiled=True)
    summed = jnp.sum(pieces.astype(jnp.float32), axis=0).astype(jnp.bfloat16)
    summed = summed.reshape(seq_count * per_dev, exp_count, part_width)
    returned = lax.all_to_all(summed, "exp", split_axis=1, concat_axis=1, tiled=True)
    recv_slots = seq_count * per_dev * exp_count
    returned = returned.reshape(recv_slots, part_width)

    recv_slot = (sender * per_dev + within) * exp_count + owner
    recv_ids = jnp.arange(recv_slots, dtype=jnp.int32)
    weights = route_weights.astype(jnp.float32)
    mix = jnp.sum(
        jnp.where(recv_slot[:, :, None] == recv_ids[None, None, :], weights[:, :, None], 0.0), axis=1
    ).astype(jnp.bfloat16)
    mixed = jnp.dot(mix, returned, preferred_element_type=jnp.float32).astype(jnp.bfloat16)

    kv_decode = kv_arrived[:, jnp.argsort(kv_slots)]
    return (mixed, kv_decode)


def solution(mesh):
    in_specs = (
        P("exp", None),
        P(),
        P("exp", None),
        P("exp", None),
        P("exp", None, "seq"),
        P("exp", None, "seq"),
        P("exp", "seq", None),
        P(None, ("seq", "exp"), None, None),
        P(("seq", "exp")),
        P(("seq", "exp")),
    )
    out_specs = (P("exp", "seq"), P(None, ("seq", "exp"), None, None))
    return jax.shard_map(
        per_device, mesh=mesh, in_specs=in_specs, out_specs=out_specs, check_vma=False
    )
```

```python
import jax
import jax.numpy as jnp
from jax import lax
from jax.sharding import PartitionSpec as P


def rms_normed(tokens, norm_gain):
    values = tokens.astype(jnp.float32)
    scale = lax.rsqrt(jnp.mean(values * values, axis=-1, keepdims=True) + 1e-06)
    return (values * scale * norm_gain).astype(jnp.bfloat16)


def route_positions(routes, experts):
    tok_count = routes.shape[0]
    expert_ids = jnp.arange(experts, dtype=jnp.int32)
    onehot = routes[:, :, None] == expert_ids[None, None, :]
    member = jnp.any(onehot, axis=1).astype(jnp.bfloat16)
    rows = jnp.arange(tok_count, dtype=jnp.int32)
    earlier = (rows[None, :] < rows[:, None]).astype(jnp.bfloat16)
    counts = jnp.dot(earlier, member, preferred_element_type=jnp.float32)
    picked = jnp.sum(jnp.where(onehot, counts[:, None, :], 0.0), axis=2)
    return picked.astype(jnp.int32)


def relayout(kv_prefill, block_map, block_empty):
    layers, blocks, block_rows, kv_width = kv_prefill.shape
    exp_count = lax.axis_size("exp")
    keep = (1 - block_empty).astype(kv_prefill.dtype)
    peer = block_map // blocks // exp_count
    target = block_map % blocks
    order = jnp.argsort(peer)
    outgoing = kv_prefill[:, order] * keep[order][None, :, None, None]
    labels = target[order]
    arrived = lax.all_to_all(outgoing, "seq", split_axis=1, concat_axis=1, tiled=True)
    slots = lax.all_to_all(labels, "seq", split_axis=0, concat_axis=0, tiled=True)
    return arrived[:, jnp.argsort(slots)]


def per_device(
    tokens,
    norm_gain,
    routes,
    route_weights,
    w_gate,
    w_up,
    w_down,
    kv_prefill,
    block_map,
    block_empty,
):
    local_experts = w_gate.shape[0]
    exp_count = lax.axis_size("exp")
    seq_count = lax.axis_size("seq")
    experts = local_experts * exp_count
    tok_count, topk = routes.shape
    capacity = tok_count * topk // experts + 1
    seq_per_expert = seq_count // local_experts
    share = capacity // seq_per_expert
    direct = capacity - share * seq_per_expert
    my_seq = lax.axis_index("seq")

    normed = rms_normed(tokens, norm_gain)
    width = normed.shape[1]

    position = route_positions(routes, experts)
    owner = routes // local_experts
    local_index = routes % local_experts
    shared = position < share * seq_per_expert
    sender = local_index * seq_per_expert + position // share
    within = position % share

    send_groups = share + local_experts * direct
    direct_group = share + local_index * direct + position - share * seq_per_expert
    slot_of = jnp.where(
        shared,
        jnp.where(sender == my_seq, within * exp_count + owner, -1),
        direct_group * exp_count + owner,
    )
    slot_ids = jnp.arange(send_groups * exp_count, dtype=jnp.int32)
    pick = jnp.any(slot_of[None, :, :] == slot_ids[:, None, None], axis=2).astype(jnp.bfloat16)
    outgoing = jnp.dot(pick, normed, preferred_element_type=jnp.float32).astype(jnp.bfloat16)
    outgoing = outgoing.reshape(send_groups, exp_count, width)
    arrived = lax.all_to_all(outgoing, "exp", split_axis=1, concat_axis=1, tiled=True)
    share_part = arrived[:share]
    copies = jnp.broadcast_to(share_part[None], (seq_count,) + share_part.shape)
    gathered = lax.all_to_all(copies, "seq", split_axis=0, concat_axis=0, tiled=True)
    share_rows = gathered.reshape(local_experts, seq_per_expert * share * exp_count, width)
    direct_rows = arrived[share:].reshape(local_experts, direct * exp_count, width)

    part_width = width // seq_count
    down = w_down.reshape(local_experts, w_down.shape[1], seq_count, part_width)

    def expert_pieces(rows):
        gate = jnp.einsum("erd,edf->erf", rows, w_gate, preferred_element_type=jnp.float32)
        upward = jnp.einsum("erd,edf->erf", rows, w_up, preferred_element_type=jnp.float32)
        hidden = (jax.nn.silu(gate) * upward).astype(jnp.bfloat16)
        return jnp.einsum(
            "erf,efcd->cerd", hidden, down, preferred_element_type=jnp.float32
        ).astype(jnp.bfloat16)

    partial_value = jnp.concatenate(
        [expert_pieces(share_rows), expert_pieces(direct_rows)], axis=2
    )
    pieces = lax.all_to_all(partial_value, "seq", split_axis=0, concat_axis=0, tiled=True)
    summed = jnp.sum(pieces.astype(jnp.float32), axis=0).astype(jnp.bfloat16)
    summed = summed.reshape(local_experts * capacity, exp_count, part_width)
    returned = lax.all_to_all(summed, "exp", split_axis=1, concat_axis=1, tiled=True)
    recv_slots = local_experts * capacity * exp_count
    returned = returned.reshape(recv_slots, part_width)

    recv_slot = (local_index * capacity + position) * exp_count + owner
    recv_ids = jnp.arange(recv_slots, dtype=jnp.int32)
    weights = route_weights.astype(jnp.float32)
    mix = jnp.sum(
        jnp.where(recv_slot[:, :, None] == recv_ids[None, None, :], weights[:, :, None], 0.0), axis=1
    ).astype(jnp.bfloat16)
    mixed = jnp.dot(mix, returned, preferred_element_type=jnp.float32).astype(jnp.bfloat16)

    kv_decode = relayout(kv_prefill, block_map, block_empty)
    return (mixed, kv_decode)


def solution(mesh):
    in_specs = (
        P("exp", None),
        P(),
        P("exp", None),
        P("exp", None),
        P("exp", None, "seq"),
        P("exp", None, "seq"),
        P("exp", "seq", None),
        P(None, ("seq", "exp"), None, None),
        P(("seq", "exp")),
        P(("seq", "exp")),
    )
    out_specs = (P("exp", "seq"), P(None, ("seq", "exp"), None, None))
    return jax.shard_map(
        per_device, mesh=mesh, in_specs=in_specs, out_specs=out_specs, check_vma=False
    )
```

```python
import jax
import jax.numpy as jnp
from jax import lax
from jax.sharding import PartitionSpec as P


def rms_normed(tokens, norm_gain):
    values = tokens.astype(jnp.float32)
    scale = lax.rsqrt(jnp.mean(values * values, axis=-1, keepdims=True) + 1e-06)
    return (values * scale * norm_gain).astype(jnp.bfloat16)


def route_positions(routes, experts):
    tok_count = routes.shape[0]
    expert_ids = jnp.arange(experts, dtype=jnp.int32)
    onehot = routes[:, :, None] == expert_ids[None, None, :]
    member = jnp.any(onehot, axis=1).astype(jnp.bfloat16)
    rows = jnp.arange(tok_count, dtype=jnp.int32)
    earlier = (rows[None, :] < rows[:, None]).astype(jnp.bfloat16)
    counts = jnp.dot(earlier, member, preferred_element_type=jnp.float32)
    picked = jnp.sum(jnp.where(onehot, counts[:, None, :], 0.0), axis=2)
    return picked.astype(jnp.int32)


def relayout(kv_prefill, block_map, block_empty):
    layers, blocks, block_rows, kv_width = kv_prefill.shape
    seq_count = lax.axis_size("seq")
    exp_count = lax.axis_size("exp")
    my_seq = lax.axis_index("seq")
    keep = (1 - block_empty).astype(kv_prefill.dtype)
    peer = block_map // blocks // exp_count
    target = block_map % blocks
    order = jnp.argsort((peer - my_seq) % seq_count)
    kept = kv_prefill[:, order] * keep[order][None, :, None, None]
    kept = jnp.transpose(kept, (1, 0, 2, 3)).reshape(blocks, -1)
    tags = jnp.broadcast_to(target[order].astype(kv_prefill.dtype)[:, None], (blocks, 128))
    outgoing = jnp.concatenate([kept, tags], axis=1)
    pieces = [outgoing[0]]
    for step in range(1, seq_count):
        route = [(i, (i + step) % seq_count) for i in range(seq_count)]
        pieces.append(lax.ppermute(outgoing[step], "seq", route))
    return jnp.stack(pieces)


def relayout_finish(arrived, kv_prefill):
    layers, blocks, block_rows, kv_width = kv_prefill.shape
    block_size = layers * block_rows * kv_width
    slots = arrived[:, block_size].astype(jnp.int32)
    placed = arrived[jnp.argsort(slots), :block_size].reshape(blocks, layers, block_rows, kv_width)
    return jnp.transpose(placed, (1, 0, 2, 3))


def per_device(
    tokens,
    norm_gain,
    routes,
    route_weights,
    w_gate,
    w_up,
    w_down,
    kv_prefill,
    block_map,
    block_empty,
):
    local_experts = w_gate.shape[0]
    exp_count = lax.axis_size("exp")
    seq_count = lax.axis_size("seq")
    experts = local_experts * exp_count
    tok_count, topk = routes.shape
    capacity = tok_count * topk // experts + 1
    seq_per_expert = seq_count // local_experts
    share = capacity // seq_per_expert
    direct = capacity - share * seq_per_expert
    my_seq = lax.axis_index("seq")

    normed = rms_normed(tokens, norm_gain)
    width = normed.shape[1]

    position = route_positions(routes, experts)
    owner = routes // local_experts
    local_index = routes % local_experts
    shared = position < share * seq_per_expert
    sender = local_index * seq_per_expert + position // share
    within = position % share

    send_groups = share + local_experts * direct
    direct_group = share + local_index * direct + position - share * seq_per_expert
    slot_of = jnp.where(
        shared,
        jnp.where(sender == my_seq, within * exp_count + owner, -1),
        direct_group * exp_count + owner,
    )
    slot_ids = jnp.arange(send_groups * exp_count, dtype=jnp.int32)
    pick = jnp.any(slot_of[None, :, :] == slot_ids[:, None, None], axis=2).astype(jnp.bfloat16)
    outgoing = jnp.dot(pick, normed, preferred_element_type=jnp.float32).astype(jnp.bfloat16)
    outgoing = outgoing.reshape(send_groups, exp_count, width)
    arrived = lax.all_to_all(outgoing, "exp", split_axis=1, concat_axis=1, tiled=True)
    kv_arrived = relayout(kv_prefill, block_map, block_empty)
    arrived, kv_arrived = lax.optimization_barrier((arrived, kv_arrived))
    share_part = arrived[:share]
    copies = jnp.broadcast_to(share_part[None], (seq_count,) + share_part.shape)
    gathered = lax.all_to_all(copies, "seq", split_axis=0, concat_axis=0, tiled=True)
    share_rows = gathered.reshape(local_experts, seq_per_expert * share * exp_count, width)
    direct_rows = arrived[share:].reshape(local_experts, direct * exp_count, width)

    part_width = width // seq_count
    down = w_down.reshape(local_experts, w_down.shape[1], seq_count, part_width)

    def expert_pieces(rows):
        gate = jnp.einsum("erd,edf->erf", rows, w_gate, preferred_element_type=jnp.float32)
        upward = jnp.einsum("erd,edf->erf", rows, w_up, preferred_element_type=jnp.float32)
        hidden = (jax.nn.silu(gate) * upward).astype(jnp.bfloat16)
        return jnp.einsum(
            "erf,efcd->cerd", hidden, down, preferred_element_type=jnp.float32
        ).astype(jnp.bfloat16)

    partial_value = jnp.concatenate(
        [expert_pieces(share_rows), expert_pieces(direct_rows)], axis=2
    )
    pieces = lax.all_to_all(partial_value, "seq", split_axis=0, concat_axis=0, tiled=True)
    summed = jnp.sum(pieces.astype(jnp.float32), axis=0).astype(jnp.bfloat16)
    summed = summed.reshape(local_experts * capacity, exp_count, part_width)
    returned = lax.all_to_all(summed, "exp", split_axis=1, concat_axis=1, tiled=True)
    recv_slots = local_experts * capacity * exp_count
    returned = returned.reshape(recv_slots, part_width)

    recv_slot = (local_index * capacity + position) * exp_count + owner
    recv_ids = jnp.arange(recv_slots, dtype=jnp.int32)
    weights = route_weights.astype(jnp.float32)
    mix = jnp.sum(
        jnp.where(recv_slot[:, :, None] == recv_ids[None, None, :], weights[:, :, None], 0.0), axis=1
    ).astype(jnp.bfloat16)
    mixed = jnp.dot(mix, returned, preferred_element_type=jnp.float32).astype(jnp.bfloat16)

    kv_decode = relayout_finish(kv_arrived, kv_prefill)
    return (mixed, kv_decode)


def solution(mesh):
    in_specs = (
        P("exp", None),
        P(),
        P("exp", None),
        P("exp", None),
        P("exp", None, "seq"),
        P("exp", None, "seq"),
        P("exp", "seq", None),
        P(None, ("seq", "exp"), None, None),
        P(("seq", "exp")),
        P(("seq", "exp")),
    )
    out_specs = (P("exp", "seq"), P(None, ("seq", "exp"), None, None))
    return jax.shard_map(
        per_device, mesh=mesh, in_specs=in_specs, out_specs=out_specs, check_vma=False
    )
```

```python
import jax
import jax.numpy as jnp
from jax import lax
from jax.sharding import PartitionSpec as P


def rms_normed(tokens, norm_gain):
    values = tokens.astype(jnp.float32)
    scale = lax.rsqrt(jnp.mean(values * values, axis=-1, keepdims=True) + 1e-06)
    return (values * scale * norm_gain).astype(jnp.bfloat16)


def route_positions(routes, experts):
    tok_count = routes.shape[0]
    expert_ids = jnp.arange(experts, dtype=jnp.int32)
    onehot = routes[:, :, None] == expert_ids[None, None, :]
    member = jnp.any(onehot, axis=1).astype(jnp.bfloat16)
    rows = jnp.arange(tok_count, dtype=jnp.int32)
    earlier = (rows[None, :] < rows[:, None]).astype(jnp.bfloat16)
    counts = jnp.dot(earlier, member, preferred_element_type=jnp.float32)
    picked = jnp.sum(jnp.where(onehot, counts[:, None, :], 0.0), axis=2)
    return picked.astype(jnp.int32)


def relayout_outgoing(kv_prefill, block_map, block_empty):
    layers, blocks, block_rows, kv_width = kv_prefill.shape
    exp_count = lax.axis_size("exp")
    keep = (1 - block_empty).astype(kv_prefill.dtype)
    peer = block_map // blocks // exp_count
    target = block_map % blocks
    order = jnp.argsort(peer)
    kept = kv_prefill[:, order] * keep[order][None, :, None, None]
    kept = jnp.transpose(kept, (1, 0, 2, 3)).reshape(blocks, -1)
    tags = jnp.broadcast_to(target[order].astype(kv_prefill.dtype)[:, None], (blocks, 128))
    return jnp.concatenate([kept, tags], axis=1)


def relayout_finish(outgoing, kv_prefill):
    layers, blocks, block_rows, kv_width = kv_prefill.shape
    block_size = layers * block_rows * kv_width
    arrived = lax.all_to_all(outgoing, "seq", split_axis=0, concat_axis=0, tiled=True)
    slots = arrived[:, block_size].astype(jnp.int32)
    place = (slots[None, :] == jnp.arange(blocks, dtype=jnp.int32)[:, None]).astype(arrived.dtype)
    data = arrived[:, :block_size].reshape(blocks, layers, block_rows, kv_width)
    return jnp.einsum(
        "ms,slrk->lmrk", place, data, preferred_element_type=jnp.float32
    ).astype(arrived.dtype)


def per_device(
    tokens,
    norm_gain,
    routes,
    route_weights,
    w_gate,
    w_up,
    w_down,
    kv_prefill,
    block_map,
    block_empty,
):
    local_experts = w_gate.shape[0]
    exp_count = lax.axis_size("exp")
    seq_count = lax.axis_size("seq")
    experts = local_experts * exp_count
    tok_count, topk = routes.shape
    capacity = tok_count * topk // experts + 1
    seq_per_expert = seq_count // local_experts
    share = capacity // seq_per_expert
    direct = capacity - share * seq_per_expert
    my_seq = lax.axis_index("seq")

    normed = rms_normed(tokens, norm_gain)
    width = normed.shape[1]

    position = route_positions(routes, experts)
    owner = routes // local_experts
    local_index = routes % local_experts
    shared = position < share * seq_per_expert
    sender = local_index * seq_per_expert + position // share
    within = position % share

    send_groups = share + local_experts * direct
    direct_group = share + local_index * direct + position - share * seq_per_expert
    slot_of = jnp.where(
        shared,
        jnp.where(sender == my_seq, within * exp_count + owner, -1),
        direct_group * exp_count + owner,
    )
    slot_ids = jnp.arange(send_groups * exp_count, dtype=jnp.int32)
    pick = jnp.any(slot_of[None, :, :] == slot_ids[:, None, None], axis=2).astype(jnp.bfloat16)
    outgoing = jnp.dot(pick, normed, preferred_element_type=jnp.float32).astype(jnp.bfloat16)
    outgoing = outgoing.reshape(send_groups, exp_count, width)
    arrived = lax.all_to_all(outgoing, "exp", split_axis=1, concat_axis=1, tiled=True)
    share_part = arrived[:share]
    copies = jnp.broadcast_to(share_part[None], (seq_count,) + share_part.shape)
    gathered = lax.all_to_all(copies, "seq", split_axis=0, concat_axis=0, tiled=True)
    kv_out = relayout_outgoing(kv_prefill, block_map, block_empty)
    gathered, kv_out = lax.optimization_barrier((gathered, kv_out))
    share_rows = gathered.reshape(local_experts, seq_per_expert * share * exp_count, width)
    direct_rows = arrived[share:].reshape(local_experts, direct * exp_count, width)

    part_width = width // seq_count
    down = w_down.reshape(local_experts, w_down.shape[1], seq_count, part_width)

    def expert_pieces(rows):
        gate = jnp.einsum("erd,edf->erf", rows, w_gate, preferred_element_type=jnp.float32)
        upward = jnp.einsum("erd,edf->erf", rows, w_up, preferred_element_type=jnp.float32)
        hidden = (jax.nn.silu(gate) * upward).astype(jnp.bfloat16)
        return jnp.einsum(
            "erf,efcd->cerd", hidden, down, preferred_element_type=jnp.float32
        ).astype(jnp.bfloat16)

    partial_value = jnp.concatenate(
        [expert_pieces(share_rows), expert_pieces(direct_rows)], axis=2
    )
    kv_decode = relayout_finish(kv_out, kv_prefill)
    kv_decode, partial_value = lax.optimization_barrier((kv_decode, partial_value))
    pieces = lax.all_to_all(partial_value, "seq", split_axis=0, concat_axis=0, tiled=True)
    summed = jnp.sum(pieces.astype(jnp.float32), axis=0).astype(jnp.bfloat16)
    summed = summed.reshape(local_experts * capacity, exp_count, part_width)
    returned = lax.all_to_all(summed, "exp", split_axis=1, concat_axis=1, tiled=True)
    recv_slots = local_experts * capacity * exp_count
    returned = returned.reshape(recv_slots, part_width)

    recv_slot = (local_index * capacity + position) * exp_count + owner
    recv_ids = jnp.arange(recv_slots, dtype=jnp.int32)
    weights = route_weights.astype(jnp.float32)
    mix = jnp.sum(
        jnp.where(recv_slot[:, :, None] == recv_ids[None, None, :], weights[:, :, None], 0.0), axis=1
    ).astype(jnp.bfloat16)
    mixed = jnp.dot(mix, returned, preferred_element_type=jnp.float32).astype(jnp.bfloat16)

    return (mixed, kv_decode)


def solution(mesh):
    in_specs = (
        P("exp", None),
        P(),
        P("exp", None),
        P("exp", None),
        P("exp", None, "seq"),
        P("exp", None, "seq"),
        P("exp", "seq", None),
        P(None, ("seq", "exp"), None, None),
        P(("seq", "exp")),
        P(("seq", "exp")),
    )
    out_specs = (P("exp", "seq"), P(None, ("seq", "exp"), None, None))
    return jax.shard_map(
        per_device, mesh=mesh, in_specs=in_specs, out_specs=out_specs, check_vma=False
    )
```

```python
import jax
import jax.numpy as jnp
from jax import lax
from jax.sharding import PartitionSpec as P


def rms_normed(tokens, norm_gain):
    values = tokens.astype(jnp.float32)
    scale = lax.rsqrt(jnp.mean(values * values, axis=-1, keepdims=True) + 1e-06)
    return (values * scale * norm_gain).astype(jnp.bfloat16)


def route_positions(routes, experts):
    tok_count = routes.shape[0]
    expert_ids = jnp.arange(experts, dtype=jnp.int32)
    onehot = routes[:, :, None] == expert_ids[None, None, :]
    member = jnp.any(onehot, axis=1).astype(jnp.bfloat16)
    rows = jnp.arange(tok_count, dtype=jnp.int32)
    earlier = (rows[None, :] < rows[:, None]).astype(jnp.bfloat16)
    counts = jnp.dot(earlier, member, preferred_element_type=jnp.float32)
    picked = jnp.sum(jnp.where(onehot, counts[:, None, :], 0.0), axis=2)
    return picked.astype(jnp.int32)


def relayout(kv_prefill, block_map, block_empty):
    layers, blocks, block_rows, kv_width = kv_prefill.shape
    exp_count = lax.axis_size("exp")
    keep = (1 - block_empty).astype(kv_prefill.dtype)
    peer = block_map // blocks // exp_count
    target = block_map % blocks
    order = jnp.argsort(peer)
    outgoing = kv_prefill[:, order] * keep[order][None, :, None, None]
    labels = target[order]
    arrived = lax.all_to_all(outgoing, "seq", split_axis=1, concat_axis=1, tiled=True)
    slots = lax.all_to_all(labels, "seq", split_axis=0, concat_axis=0, tiled=True)
    return arrived[:, jnp.argsort(slots)]


def per_device(
    tokens,
    norm_gain,
    routes,
    route_weights,
    w_gate,
    w_up,
    w_down,
    kv_prefill,
    block_map,
    block_empty,
):
    local_experts = w_gate.shape[0]
    exp_count = lax.axis_size("exp")
    seq_count = lax.axis_size("seq")
    experts = local_experts * exp_count
    tok_count, topk = routes.shape
    capacity = tok_count * topk // experts + 1
    share = capacity // seq_count
    direct = capacity - share * seq_count
    my_seq = lax.axis_index("seq")

    normed = rms_normed(tokens, norm_gain)
    width = normed.shape[1]

    position = route_positions(routes, experts)
    owner = routes // local_experts
    local_index = routes % local_experts
    shared = position < share * seq_count
    sender = position // share
    within = position % share

    share_groups = local_experts * share
    send_groups = share_groups + local_experts * direct
    direct_group = share_groups + local_index * direct + position - share * seq_count
    slot_of = jnp.where(
        shared,
        jnp.where(sender == my_seq, (local_index * share + within) * exp_count + owner, -1),
        direct_group * exp_count + owner,
    )
    slot_ids = jnp.arange(send_groups * exp_count, dtype=jnp.int32)
    pick = jnp.any(slot_of[None, :, :] == slot_ids[:, None, None], axis=2).astype(jnp.bfloat16)
    outgoing = jnp.dot(pick, normed, preferred_element_type=jnp.float32).astype(jnp.bfloat16)
    outgoing = outgoing.reshape(send_groups, exp_count, width)
    arrived = lax.all_to_all(outgoing, "exp", split_axis=1, concat_axis=1, tiled=True)

    part_width = width // seq_count

    def expert_pieces(rows, e):
        gate = jnp.dot(rows, w_gate[e], preferred_element_type=jnp.float32)
        upward = jnp.dot(rows, w_up[e], preferred_element_type=jnp.float32)
        hidden = (jax.nn.silu(gate) * upward).astype(jnp.bfloat16)
        down = w_down[e].reshape(w_down.shape[1], seq_count, part_width)
        return jnp.einsum(
            "rf,fcd->crd", hidden, down, preferred_element_type=jnp.float32
        ).astype(jnp.bfloat16)

    totals = []
    for e in range(local_experts):
        share_part = arrived[e * share:(e + 1) * share]
        copies = jnp.broadcast_to(share_part[None], (seq_count,) + share_part.shape)
        gathered = lax.all_to_all(copies, "seq", split_axis=0, concat_axis=0, tiled=True)
        share_rows = gathered.reshape(seq_count * share * exp_count, width)
        direct_rows = arrived[share_groups + e * direct:share_groups + (e + 1) * direct]
        direct_rows = direct_rows.reshape(direct * exp_count, width)
        partial_value = jnp.concatenate(
            [expert_pieces(share_rows, e), expert_pieces(direct_rows, e)], axis=1
        )
        pieces = lax.all_to_all(partial_value, "seq", split_axis=0, concat_axis=0, tiled=True)
        totals.append(jnp.sum(pieces.astype(jnp.float32), axis=0).astype(jnp.bfloat16))
    summed = jnp.stack(totals).reshape(local_experts * capacity, exp_count, part_width)
    returned = lax.all_to_all(summed, "exp", split_axis=1, concat_axis=1, tiled=True)
    recv_slots = local_experts * capacity * exp_count
    returned = returned.reshape(recv_slots, part_width)

    recv_slot = (local_index * capacity + position) * exp_count + owner
    recv_ids = jnp.arange(recv_slots, dtype=jnp.int32)
    weights = route_weights.astype(jnp.float32)
    mix = jnp.sum(
        jnp.where(recv_slot[:, :, None] == recv_ids[None, None, :], weights[:, :, None], 0.0), axis=1
    ).astype(jnp.bfloat16)
    mixed = jnp.dot(mix, returned, preferred_element_type=jnp.float32).astype(jnp.bfloat16)

    kv_decode = relayout(kv_prefill, block_map, block_empty)
    return (mixed, kv_decode)


def solution(mesh):
    in_specs = (
        P("exp", None),
        P(),
        P("exp", None),
        P("exp", None),
        P("exp", None, "seq"),
        P("exp", None, "seq"),
        P("exp", "seq", None),
        P(None, ("seq", "exp"), None, None),
        P(("seq", "exp")),
        P(("seq", "exp")),
    )
    out_specs = (P("exp", "seq"), P(None, ("seq", "exp"), None, None))
    return jax.shard_map(
        per_device, mesh=mesh, in_specs=in_specs, out_specs=out_specs, check_vma=False
    )
```

```python
import jax
import jax.numpy as jnp
from jax import lax
from jax.sharding import PartitionSpec as P


def rms_normed(tokens, norm_gain):
    values = tokens.astype(jnp.float32)
    scale = lax.rsqrt(jnp.mean(values * values, axis=-1, keepdims=True) + 1e-06)
    return (values * scale * norm_gain).astype(jnp.bfloat16)


def route_positions(routes, experts):
    tok_count = routes.shape[0]
    expert_ids = jnp.arange(experts, dtype=jnp.int32)
    onehot = routes[:, :, None] == expert_ids[None, None, :]
    member = jnp.any(onehot, axis=1).astype(jnp.bfloat16)
    rows = jnp.arange(tok_count, dtype=jnp.int32)
    earlier = (rows[None, :] < rows[:, None]).astype(jnp.bfloat16)
    counts = jnp.dot(earlier, member, preferred_element_type=jnp.float32)
    picked = jnp.sum(jnp.where(onehot, counts[:, None, :], 0.0), axis=2)
    return picked.astype(jnp.int32)


def relayout(kv_prefill, block_map, block_empty):
    layers, blocks, block_rows, kv_width = kv_prefill.shape
    exp_count = lax.axis_size("exp")
    keep = (1 - block_empty).astype(kv_prefill.dtype)
    peer = block_map // blocks // exp_count
    target = block_map % blocks
    order = jnp.argsort(peer)
    kept = kv_prefill[:, order] * keep[order][None, :, None, None]
    tags = jnp.broadcast_to(
        target[order].astype(kv_prefill.dtype)[None, :, None, None], (layers, blocks, block_rows, 128)
    )
    outgoing = jnp.concatenate([kept, tags], axis=3)
    arrived = lax.all_to_all(outgoing, "seq", split_axis=1, concat_axis=1, tiled=True)
    slots = arrived[0, :, 0, kv_width].astype(jnp.int32)
    data = lax.slice_in_dim(arrived, 0, kv_width, axis=3)
    return jnp.take(data, jnp.argsort(slots), axis=1)


def per_device(
    tokens,
    norm_gain,
    routes,
    route_weights,
    w_gate,
    w_up,
    w_down,
    kv_prefill,
    block_map,
    block_empty,
):
    local_experts = w_gate.shape[0]
    exp_count = lax.axis_size("exp")
    seq_count = lax.axis_size("seq")
    experts = local_experts * exp_count
    tok_count, topk = routes.shape
    capacity = tok_count * topk // experts + 1
    share = capacity // seq_count
    direct = capacity - share * seq_count
    my_seq = lax.axis_index("seq")

    normed = rms_normed(tokens, norm_gain)
    width = normed.shape[1]

    position = route_positions(routes, experts)
    owner = routes // local_experts
    local_index = routes % local_experts
    shared = position < share * seq_count
    sender = position // share
    within = position % share

    share_groups = local_experts * share
    send_groups = share_groups + local_experts * direct
    direct_group = share_groups + local_index * direct + position - share * seq_count
    slot_of = jnp.where(
        shared,
        jnp.where(sender == my_seq, (local_index * share + within) * exp_count + owner, -1),
        direct_group * exp_count + owner,
    )
    slot_ids = jnp.arange(send_groups * exp_count, dtype=jnp.int32)
    pick = jnp.any(slot_of[None, :, :] == slot_ids[:, None, None], axis=2).astype(jnp.bfloat16)
    outgoing = jnp.dot(pick, normed, preferred_element_type=jnp.float32).astype(jnp.bfloat16)
    outgoing = outgoing.reshape(send_groups, exp_count, width)
    arrived = lax.all_to_all(outgoing, "exp", split_axis=1, concat_axis=1, tiled=True)

    part_width = width // seq_count

    def expert_pieces(rows, e):
        gate = jnp.dot(rows, w_gate[e], preferred_element_type=jnp.float32)
        upward = jnp.dot(rows, w_up[e], preferred_element_type=jnp.float32)
        hidden = (jax.nn.silu(gate) * upward).astype(jnp.bfloat16)
        down = w_down[e].reshape(w_down.shape[1], seq_count, part_width)
        return jnp.einsum(
            "rf,fcd->crd", hidden, down, preferred_element_type=jnp.float32
        ).astype(jnp.bfloat16)

    totals = []
    for e in range(local_experts):
        share_part = arrived[e * share:(e + 1) * share]
        copies = jnp.broadcast_to(share_part[None], (seq_count,) + share_part.shape)
        gathered = lax.all_to_all(copies, "seq", split_axis=0, concat_axis=0, tiled=True)
        share_rows = gathered.reshape(seq_count * share * exp_count, width)
        direct_rows = arrived[share_groups + e * direct:share_groups + (e + 1) * direct]
        direct_rows = direct_rows.reshape(direct * exp_count, width)
        partial_value = jnp.concatenate(
            [expert_pieces(share_rows, e), expert_pieces(direct_rows, e)], axis=1
        )
        pieces = lax.all_to_all(partial_value, "seq", split_axis=0, concat_axis=0, tiled=True)
        totals.append(jnp.sum(pieces.astype(jnp.float32), axis=0).astype(jnp.bfloat16))
    summed = jnp.stack(totals).reshape(local_experts * capacity, exp_count, part_width)
    returned = lax.all_to_all(summed, "exp", split_axis=1, concat_axis=1, tiled=True)
    recv_slots = local_experts * capacity * exp_count
    returned = returned.reshape(recv_slots, part_width)

    recv_slot = (local_index * capacity + position) * exp_count + owner
    recv_ids = jnp.arange(recv_slots, dtype=jnp.int32)
    weights = route_weights.astype(jnp.float32)
    mix = jnp.sum(
        jnp.where(recv_slot[:, :, None] == recv_ids[None, None, :], weights[:, :, None], 0.0), axis=1
    ).astype(jnp.bfloat16)
    mixed = jnp.dot(mix, returned, preferred_element_type=jnp.float32).astype(jnp.bfloat16)

    kv_decode = relayout(kv_prefill, block_map, block_empty)
    return (mixed, kv_decode)


def solution(mesh):
    in_specs = (
        P("exp", None),
        P(),
        P("exp", None),
        P("exp", None),
        P("exp", None, "seq"),
        P("exp", None, "seq"),
        P("exp", "seq", None),
        P(None, ("seq", "exp"), None, None),
        P(("seq", "exp")),
        P(("seq", "exp")),
    )
    out_specs = (P("exp", "seq"), P(None, ("seq", "exp"), None, None))
    return jax.shard_map(
        per_device, mesh=mesh, in_specs=in_specs, out_specs=out_specs, check_vma=False
    )
```

```python
import jax
import jax.numpy as jnp
from jax import lax
from jax.sharding import PartitionSpec as P


def rms_normed(tokens, norm_gain):
    values = tokens.astype(jnp.float32)
    scale = lax.rsqrt(jnp.mean(values * values, axis=-1, keepdims=True) + 1e-06)
    return (values * scale * norm_gain).astype(jnp.bfloat16)


def route_positions(routes, experts):
    tok_count = routes.shape[0]
    expert_ids = jnp.arange(experts, dtype=jnp.int32)
    onehot = routes[:, :, None] == expert_ids[None, None, :]
    member = jnp.any(onehot, axis=1).astype(jnp.bfloat16)
    rows = jnp.arange(tok_count, dtype=jnp.int32)
    earlier = (rows[None, :] < rows[:, None]).astype(jnp.bfloat16)
    counts = jnp.dot(earlier, member, preferred_element_type=jnp.float32)
    picked = jnp.sum(jnp.where(onehot, counts[:, None, :], 0.0), axis=2)
    return picked.astype(jnp.int32)


def relayout(kv_prefill, block_map, block_empty):
    layers, blocks, block_rows, kv_width = kv_prefill.shape
    seq_count = lax.axis_size("seq")
    exp_count = lax.axis_size("exp")
    my_seq = lax.axis_index("seq")
    keep = (1 - block_empty).astype(kv_prefill.dtype)
    peer = block_map // blocks // exp_count
    target = block_map % blocks
    order = jnp.argsort((peer - my_seq) % seq_count)
    kept = kv_prefill[:, order] * keep[order][None, :, None, None]
    tags = jnp.broadcast_to(
        target[order].astype(kv_prefill.dtype)[None, :, None, None], (layers, blocks, block_rows, 128)
    )
    outgoing = jnp.concatenate([kept, tags], axis=3)
    pieces = [outgoing[:, 0]]
    for step in range(1, seq_count):
        route = [(i, (i + step) % seq_count) for i in range(seq_count)]
        pieces.append(lax.ppermute(outgoing[:, step], "seq", route))
    return jnp.stack(pieces, axis=1)


def relayout_finish(arrived, kv_width):
    slots = arrived[0, :, 0, kv_width].astype(jnp.int32)
    data = lax.slice_in_dim(arrived, 0, kv_width, axis=3)
    return jnp.take(data, jnp.argsort(slots), axis=1)


def per_device(
    tokens,
    norm_gain,
    routes,
    route_weights,
    w_gate,
    w_up,
    w_down,
    kv_prefill,
    block_map,
    block_empty,
):
    local_experts = w_gate.shape[0]
    exp_count = lax.axis_size("exp")
    seq_count = lax.axis_size("seq")
    experts = local_experts * exp_count
    tok_count, topk = routes.shape
    capacity = tok_count * topk // experts + 1
    share = capacity // seq_count
    direct = capacity - share * seq_count
    my_seq = lax.axis_index("seq")

    normed = rms_normed(tokens, norm_gain)
    width = normed.shape[1]

    position = route_positions(routes, experts)
    owner = routes // local_experts
    local_index = routes % local_experts
    shared = position < share * seq_count
    sender = position // share
    within = position % share

    share_groups = local_experts * share
    send_groups = share_groups + local_experts * direct
    direct_group = share_groups + local_index * direct + position - share * seq_count
    slot_of = jnp.where(
        shared,
        jnp.where(sender == my_seq, (local_index * share + within) * exp_count + owner, -1),
        direct_group * exp_count + owner,
    )
    slot_ids = jnp.arange(send_groups * exp_count, dtype=jnp.int32)
    pick = jnp.any(slot_of[None, :, :] == slot_ids[:, None, None], axis=2).astype(jnp.bfloat16)
    outgoing = jnp.dot(pick, normed, preferred_element_type=jnp.float32).astype(jnp.bfloat16)
    outgoing = outgoing.reshape(send_groups, exp_count, width)
    arrived = lax.all_to_all(outgoing, "exp", split_axis=1, concat_axis=1, tiled=True)
    kv_arrived = relayout(kv_prefill, block_map, block_empty)
    arrived, kv_arrived = lax.optimization_barrier((arrived, kv_arrived))

    part_width = width // seq_count

    def expert_pieces(rows, e):
        gate = jnp.dot(rows, w_gate[e], preferred_element_type=jnp.float32)
        upward = jnp.dot(rows, w_up[e], preferred_element_type=jnp.float32)
        hidden = (jax.nn.silu(gate) * upward).astype(jnp.bfloat16)
        down = w_down[e].reshape(w_down.shape[1], seq_count, part_width)
        return jnp.einsum(
            "rf,fcd->crd", hidden, down, preferred_element_type=jnp.float32
        ).astype(jnp.bfloat16)

    totals = []
    for e in range(local_experts):
        share_part = arrived[e * share:(e + 1) * share]
        copies = jnp.broadcast_to(share_part[None], (seq_count,) + share_part.shape)
        gathered = lax.all_to_all(copies, "seq", split_axis=0, concat_axis=0, tiled=True)
        share_rows = gathered.reshape(seq_count * share * exp_count, width)
        direct_rows = arrived[share_groups + e * direct:share_groups + (e + 1) * direct]
        direct_rows = direct_rows.reshape(direct * exp_count, width)
        partial_value = jnp.concatenate(
            [expert_pieces(share_rows, e), expert_pieces(direct_rows, e)], axis=1
        )
        pieces = lax.all_to_all(partial_value, "seq", split_axis=0, concat_axis=0, tiled=True)
        totals.append(jnp.sum(pieces.astype(jnp.float32), axis=0).astype(jnp.bfloat16))
    summed = jnp.stack(totals).reshape(local_experts * capacity, exp_count, part_width)
    returned = lax.all_to_all(summed, "exp", split_axis=1, concat_axis=1, tiled=True)
    recv_slots = local_experts * capacity * exp_count
    returned = returned.reshape(recv_slots, part_width)

    recv_slot = (local_index * capacity + position) * exp_count + owner
    recv_ids = jnp.arange(recv_slots, dtype=jnp.int32)
    weights = route_weights.astype(jnp.float32)
    mix = jnp.sum(
        jnp.where(recv_slot[:, :, None] == recv_ids[None, None, :], weights[:, :, None], 0.0), axis=1
    ).astype(jnp.bfloat16)
    mixed = jnp.dot(mix, returned, preferred_element_type=jnp.float32).astype(jnp.bfloat16)

    kv_decode = relayout_finish(kv_arrived, kv_prefill.shape[3])
    return (mixed, kv_decode)


def solution(mesh):
    in_specs = (
        P("exp", None),
        P(),
        P("exp", None),
        P("exp", None),
        P("exp", None, "seq"),
        P("exp", None, "seq"),
        P("exp", "seq", None),
        P(None, ("seq", "exp"), None, None),
        P(("seq", "exp")),
        P(("seq", "exp")),
    )
    out_specs = (P("exp", "seq"), P(None, ("seq", "exp"), None, None))
    return jax.shard_map(
        per_device, mesh=mesh, in_specs=in_specs, out_specs=out_specs, check_vma=False
    )
```

```python
import jax
import jax.numpy as jnp
from jax import lax
from jax.sharding import PartitionSpec as P


def rms_normed(tokens, norm_gain):
    values = tokens.astype(jnp.float32)
    scale = lax.rsqrt(jnp.mean(values * values, axis=-1, keepdims=True) + 1e-06)
    return (values * scale * norm_gain).astype(jnp.bfloat16)


def route_positions(routes, experts):
    tok_count = routes.shape[0]
    expert_ids = jnp.arange(experts, dtype=jnp.int32)
    onehot = routes[:, :, None] == expert_ids[None, None, :]
    member = jnp.any(onehot, axis=1).astype(jnp.bfloat16)
    rows = jnp.arange(tok_count, dtype=jnp.int32)
    earlier = (rows[None, :] < rows[:, None]).astype(jnp.bfloat16)
    counts = jnp.dot(earlier, member, preferred_element_type=jnp.float32)
    picked = jnp.sum(jnp.where(onehot, counts[:, None, :], 0.0), axis=2)
    return picked.astype(jnp.int32)


def relayout(kv_prefill, block_map, block_empty):
    layers, blocks, block_rows, _ = kv_prefill.shape
    seq_count = lax.axis_size("seq")
    exp_count = lax.axis_size("exp")
    my_seq = lax.axis_index("seq")
    keep = (1 - block_empty).astype(kv_prefill.dtype)
    peer = block_map // blocks // exp_count
    target = block_map % blocks
    order = jnp.argsort((peer - my_seq) % seq_count)
    kept = kv_prefill[:, order] * keep[order][None, :, None, None]
    tags = jnp.broadcast_to(
        target[order].astype(kv_prefill.dtype)[None, :, None, None], (layers, blocks, block_rows, 128)
    )
    outgoing = jnp.concatenate([kept, tags], axis=3)
    pieces = [outgoing[:, 0]]
    for step in range(1, seq_count):
        route = [(i, (i + step) % seq_count) for i in range(seq_count)]
        pieces.append(lax.ppermute(outgoing[:, step], "seq", route))
    return jnp.stack(pieces, axis=1)


def relayout_finish(arrived, kv_width):
    slots = arrived[0, :, 0, kv_width].astype(jnp.int32)
    data = lax.slice_in_dim(arrived, 0, kv_width, axis=3)
    return jnp.take(data, jnp.argsort(slots), axis=1)


def layer(
    tokens,
    norm_gain,
    routes,
    route_weights,
    w_gate,
    w_up,
    w_down,
    kv_prefill,
    block_map,
    block_empty,
):
    local_experts = w_gate.shape[0]
    exp_count = lax.axis_size("exp")
    seq_count = lax.axis_size("seq")
    experts = local_experts * exp_count
    tok_count, topk = routes.shape
    capacity = tok_count * topk // experts + 1
    share = capacity // seq_count
    direct = capacity - share * seq_count
    my_seq = lax.axis_index("seq")

    normed = rms_normed(tokens, norm_gain)
    width = normed.shape[1]

    position = route_positions(routes, experts)
    owner = routes // local_experts
    local_index = routes % local_experts
    shared = position < share * seq_count
    sender = position // share
    within = position % share

    share_groups = local_experts * share
    send_groups = share_groups + local_experts * direct
    direct_group = share_groups + local_index * direct + position - share * seq_count
    slot_of = jnp.where(
        shared,
        jnp.where(sender == my_seq, (local_index * share + within) * exp_count + owner, -1),
        direct_group * exp_count + owner,
    )
    slot_ids = jnp.arange(send_groups * exp_count, dtype=jnp.int32)
    pick = jnp.any(slot_of[None, :, :] == slot_ids[:, None, None], axis=2).astype(jnp.bfloat16)
    outgoing = jnp.dot(pick, normed, preferred_element_type=jnp.float32).astype(jnp.bfloat16)
    outgoing = outgoing.reshape(send_groups, exp_count, width)
    arrived = lax.all_to_all(outgoing, "exp", split_axis=1, concat_axis=1, tiled=True)

    part_width = width // seq_count

    def expert_pieces(rows, e):
        gate = jnp.dot(rows, w_gate[e], preferred_element_type=jnp.float32)
        upward = jnp.dot(rows, w_up[e], preferred_element_type=jnp.float32)
        hidden = (jax.nn.silu(gate) * upward).astype(jnp.bfloat16)
        down = w_down[e].reshape(w_down.shape[1], seq_count, part_width)
        return jnp.einsum(
            "rf,fcd->crd", hidden, down, preferred_element_type=jnp.float32
        ).astype(jnp.bfloat16)

    totals = []
    for e in range(local_experts):
        share_part = arrived[e * share:(e + 1) * share]
        copies = jnp.broadcast_to(share_part[None], (seq_count,) + share_part.shape)
        gathered = lax.all_to_all(copies, "seq", split_axis=0, concat_axis=0, tiled=True)
        share_rows = gathered.reshape(seq_count * share * exp_count, width)
        direct_rows = arrived[share_groups + e * direct:share_groups + (e + 1) * direct]
        direct_rows = direct_rows.reshape(direct * exp_count, width)
        partial_value = jnp.concatenate(
            [expert_pieces(share_rows, e), expert_pieces(direct_rows, e)], axis=1
        )
        pieces = lax.all_to_all(partial_value, "seq", split_axis=0, concat_axis=0, tiled=True)
        totals.append(jnp.sum(pieces.astype(jnp.float32), axis=0).astype(jnp.bfloat16))
    summed = jnp.stack(totals).reshape(local_experts * capacity, exp_count, part_width)
    kv_prefill, summed = lax.optimization_barrier((kv_prefill, summed))
    returned = lax.all_to_all(summed, "exp", split_axis=1, concat_axis=1, tiled=True)
    kv_arrived = relayout(kv_prefill, block_map, block_empty)
    recv_slots = local_experts * capacity * exp_count
    returned = returned.reshape(recv_slots, part_width)

    recv_slot = (local_index * capacity + position) * exp_count + owner
    recv_ids = jnp.arange(recv_slots, dtype=jnp.int32)
    weights = route_weights.astype(jnp.float32)
    mix = jnp.sum(
        jnp.where(recv_slot[:, :, None] == recv_ids[None, None, :], weights[:, :, None], 0.0), axis=1
    ).astype(jnp.bfloat16)
    mixed = jnp.dot(mix, returned, preferred_element_type=jnp.float32).astype(jnp.bfloat16)

    kv_decode = relayout_finish(kv_arrived, kv_prefill.shape[3])
    return (mixed, kv_decode)


def solution(mesh):
    in_specs = (
        P("exp", None),
        P(),
        P("exp", None),
        P("exp", None),
        P("exp", None, "seq"),
        P("exp", None, "seq"),
        P("exp", "seq", None),
        P(None, ("seq", "exp"), None, None),
        P(("seq", "exp")),
        P(("seq", "exp")),
    )
    out_specs = (P("exp", "seq"), P(None, ("seq", "exp"), None, None))
    return jax.shard_map(layer, mesh=mesh, in_specs=in_specs, out_specs=out_specs, check_vma=False)
```
